32 devices in a mesh: groups: 2 (over y), span: 4 (over z), layer: 2 (over x), rep: 2 (over core).
Axes of the slice: x: 2, y: 2, z: 4, core: 2. Of those that a mesh axis runs over, the one named last changes fastest.
Arguments:
- queries: bfloat16 [4096, 2, 4096], P('groups', 'layer', 'span'), parts along dimension 0, may hold values from -6 to 6
- train_grads: bfloat16 [4096, 2, 4096], P(('groups', 'span'), 'layer'), parts along dimension 0, may hold values from -6 to 6
- precond: float32 [2, 4096], P('layer', 'span'), may hold values from 0.25 to 4
- requests: int32 [8, 6], P('groups'), parts along dimension 0, may hold values from 0 to 15, as said below
- pair_slot: int32 [8, 24], P(('groups', 'span')), parts along dimension 0, may hold values from 0 to 5
- pair_train: int32 [8, 24], P(('groups', 'span')), parts along dimension 0, may hold values from 0 to 3
- pair_count: int32 [8, 2], P(('groups', 'span')), parts along dimension 0, may hold values from 1 to 12, as said below
Outputs:
- scores: float32 [8, 3072, 128], P(('groups', 'span'), ('layer', 'rep')), parts along dimension 0
The draws below stay inside these ranges and needn't reach their ends.
There are 2 independent parts, one for each index of `groups`. The reference program is written for one: setup_inputs(seed, part) draws one part's arguments, and reference() takes and returns one part's arrays. A program takes and returns all parts, laid end to end along the dimension named above; an argument that names none is the same for every part. Nothing has to cross between parts.
Inputs may be any that keep to these rules, and one draw needn't show every extreme that they name: `requests`: each row names 6 different query blocks. The live pairs of half h of shard c's list are the first pair_count[c, h] of that half's 12 slots; some half is full in every draw.
All inputs are finite; a program needn't handle non-finite values.
Results may differ from the reference program's by a relative error of at most 0.0029.
Values may be sent and summed in bfloat16 or wider, within the bound.
No kernel may reach another device: no remote copies, remote signals or barrier semaphores. Data moves between devices by JAX's collectives and lax.ppermute only.
A program may use at most 64 MiB of HBM per device.

```python
import math
import jax
import jax.numpy as jnp
from jax import lax

D = 4096
BLOCK = 128
NQ = 2048
CAP = 6
PHALF = 12
TB_DEV = 4
PMAX = 24
L = 2
NTRAIN = 2048
N_SPAN = 4


def draw_requests(key, part):
    row_keys = jax.random.split(jax.random.fold_in(key, 11), N_SPAN)

    def draw_row(row_key):
        return jax.random.permutation(row_key, NQ // BLOCK)[:CAP]
    return jax.vmap(draw_row)(row_keys).astype(jnp.int32)


def draw_pair_count(key, part):
    key_light, key_heavy, key_level, key_chosen = jax.random.split(jax.random.fold_in(key, 23), 4)
    light_counts = jax.random.randint(key_light, (N_SPAN, 2), 1, PHALF // 2 + 1)
    heavy_mask = jax.random.randint(key_heavy, (N_SPAN, 2), 0, 8) == 0
    heavy_counts = jax.random.randint(key_level, (N_SPAN, 2), PHALF // 2 + 1, PHALF + 1)
    mixed_counts = jnp.where(heavy_mask, heavy_counts, light_counts).reshape(-1)
    chosen = jax.random.randint(key_chosen, (), 0, N_SPAN * 2)
    flattened = jnp.where(jnp.arange(N_SPAN * 2) == chosen, PHALF, mixed_counts)
    return flattened.reshape(N_SPAN, 2).astype(jnp.int32)


def set_ends(drawn, rng, smallest, high):
    extent = drawn.shape
    spot = [jax.random.randint(jax.random.fold_in(rng, axis), (), 0, extent[axis]) for axis in range(len(extent))]
    drawn = drawn.at[tuple(spot)].set(smallest)
    longest = extent.index(max(extent))
    spot[longest] = (spot[longest] + 1) % extent[longest]
    return drawn.at[tuple(spot)].set(high)


def level_of(own_key, extent, cuts, smallest, high):
    level, own = 1.0, jax.random.fold_in(own_key, 6)
    for position, blocks in cuts:
        heights = jnp.exp(jax.random.uniform(jax.random.fold_in(own, position), (blocks,), jnp.float32, smallest / len(cuts), high / len(cuts)))
        level = level * jnp.repeat(heights, extent[position] // blocks).reshape([-1 if axis == position else 1 for axis in range(len(extent))])
    return level


def gaussian(stream_key, extent, width, limit, cuts=(), kind=jnp.bfloat16):
    drawn = jax.random.normal(stream_key, extent, jnp.float32) * width
    if len(cuts) > 0:
        drawn = level_of(stream_key, extent, cuts, -0.22, 0.18) * drawn
    return jnp.clip(drawn, min=-limit, max=limit).astype(kind)


def setup_inputs(seed: int = 0, part: int = 0) -> dict:
    streams_of = jax.random.split(jax.random.key(seed), 8)
    own_keys = jax.random.split(jax.random.fold_in(streams_of[7], part), 8)
    queries = gaussian(own_keys[0], (NQ, L, D), 1.0, 6.0, ((1, 2), (2, 4)))
    train_grads = gaussian(own_keys[1], (NTRAIN, L, D), 1.0, 6.0, ((0, 4), (1, 2)))
    precond = jnp.clip(jnp.exp(math.log(4.0) - 2.7725887 * jax.random.uniform(streams_of[2], (L, D), jnp.float32) ** level_of(streams_of[2], (L, D), ((0, 2), (1, 4)), -0.2, 0.2)), 0.25, 4.0)
    requests = draw_requests(jax.random.fold_in(jax.random.fold_in(streams_of[7], part), 71), part)
    pair_slot = set_ends(jax.random.randint(own_keys[4], (N_SPAN, PMAX), 0, CAP), jax.random.fold_in(own_keys[4], 1), 0, CAP - 1).astype(jnp.int32)
    pair_train = set_ends(jax.random.randint(own_keys[5], (N_SPAN, PMAX), 0, TB_DEV), jax.random.fold_in(own_keys[5], 1), 0, TB_DEV - 1).astype(jnp.int32)
    pair_count = draw_pair_count(jax.random.fold_in(jax.random.fold_in(streams_of[7], part), 71), part)
    return {"queries": queries, "train_grads": train_grads, "precond": precond, "requests": requests, "pair_slot": pair_slot, "pair_train": pair_train, "pair_count": pair_count}


def reference(queries, train_grads, precond, requests, pair_slot, pair_train, pair_count):
    prepared = (queries.astype(jnp.float32) * precond[None]).astype(jnp.bfloat16)
    query_blocks = prepared.reshape(NQ // BLOCK, BLOCK, L, D)
    train_blocks = train_grads.reshape(N_SPAN * TB_DEV, BLOCK, L, D)
    score_scale = 1.0 / math.sqrt(L * D)
    owners = jnp.repeat(jnp.arange(N_SPAN, dtype=jnp.int32), PMAX)
    slot_ids = jnp.tile(jnp.arange(PMAX, dtype=jnp.int32), N_SPAN)

    def score_pair(pair_item):
        owner_index, slot_index = pair_item
        query_block = requests[owner_index, pair_slot[owner_index, slot_index]]
        train_block = owner_index * TB_DEV + pair_train[owner_index, slot_index]
        is_live = slot_index % PHALF < pair_count[owner_index, slot_index // PHALF]
        query_tile = query_blocks[query_block].astype(jnp.float32)
        train_tile = train_blocks[train_block].astype(jnp.float32)
        partial_value = jnp.einsum('ild,jld->ij', query_tile, train_tile, precision=lax.Precision.HIGHEST) * score_scale
        return jnp.where(is_live, partial_value, jnp.zeros_like(partial_value))
    all_blocks = lax.map(score_pair, (owners, slot_ids))
    return all_blocks.reshape(N_SPAN, PMAX * BLOCK, BLOCK)
```

```python
import math

import jax
import jax.numpy as jnp
from jax import lax
from jax.sharding import PartitionSpec as P

BLOCK = 128


def shards(queries, train_grads, precond, requests, pair_slot, pair_train, pair_count):
    n_query, l_dev, features = queries.shape
    n_span = lax.axis_size("span")
    n_rep = lax.axis_size("rep")
    d_full = train_grads.shape[2]
    tb_dev = train_grads.shape[0] // BLOCK
    pmax = pair_slot.shape[1]
    cap = requests.shape[1]
    phalf = pmax // pair_count.shape[1]
    half = features // n_rep
    rep_index = lax.axis_index("rep")

    q_half = lax.dynamic_slice_in_dim(queries, rep_index * half, half, axis=2)
    p_half = lax.dynamic_slice_in_dim(precond, rep_index * half, half, axis=1)
    q_blocks = q_half.reshape(n_query // BLOCK, BLOCK, l_dev, half)
    picked = q_blocks[requests.reshape(-1)]
    picked = (picked.astype(jnp.float32) * p_half[None, None]).astype(jnp.bfloat16)
    picked = picked.reshape(n_span, cap, BLOCK, l_dev, half)
    arrived = lax.all_to_all(picked, "span", split_axis=0, concat_axis=0, tiled=True)

    train = train_grads.reshape(tb_dev, BLOCK, l_dev, n_span, n_rep, half)
    train = lax.dynamic_index_in_dim(train, rep_index, axis=4, keepdims=False)

    combos = lax.dot_general(
        arrived,
        train,
        (((0, 3, 4), (3, 2, 4)), ((), ())),
        preferred_element_type=jnp.float32,
    )
    score_scale = 1.0 / math.sqrt(l_dev * lax.axis_size("layer") * d_full)
    combos = jnp.transpose(combos, (0, 2, 1, 3)).reshape(cap * tb_dev, BLOCK, BLOCK)
    slot_row = pair_slot[0]
    train_row = pair_train[0]
    counts = pair_count[0]
    chosen = combos[slot_row * tb_dev + train_row] * score_scale
    slots = jnp.arange(pmax, dtype=jnp.int32)
    live = (slots % phalf) < counts[slots // phalf]
    partials = jnp.where(live[:, None, None], chosen, 0.0).reshape(pmax * BLOCK, BLOCK)
    summed = lax.psum_scatter(partials, ("layer", "rep"), scatter_dimension=0, tiled=True)
    return summed[None]


def solution(mesh):
    placed = (
        P("groups", "layer", "span"),
        P(("groups", "span"), "layer", None),
        P("layer", "span"),
        P("groups", None),
        P(("groups", "span"), None),
        P(("groups", "span"), None),
        P(("groups", "span"), None),
    )
    return jax.shard_map(
        shards,
        mesh=mesh,
        in_specs=placed,
        out_specs=P(("groups", "span"), ("layer", "rep"), None),
        check_vma=False,
    )
```

```python
import math

import jax
import jax.numpy as jnp
from jax import lax
from jax.sharding import PartitionSpec as P

BLOCK = 128
ROW_CHUNKS = 2


def ring_reduce_scatter(x, axis_name, dim):
    n = lax.axis_size(axis_name)
    me = lax.axis_index(axis_name)

    def piece(c):
        return lax.dynamic_index_in_dim(x, c % n, axis=dim, keepdims=False)

    if n == 1:
        return piece(me)
    perm = [(i, (i + 1) % n) for i in range(n)]
    acc = piece(me - 1 + n)
    for t in range(n - 1):
        recv = lax.ppermute(acc, axis_name, perm)
        acc = recv + piece(me - 2 - t + 2 * n)
    return acc


def shards(queries, train_grads, precond, requests, pair_slot, pair_train, pair_count):
    n_query, l_dev, features = queries.shape
    n_span = lax.axis_size("span")
    n_rep = lax.axis_size("rep")
    n_layer = lax.axis_size("layer")
    d_full = train_grads.shape[2]
    tb_dev = train_grads.shape[0] // BLOCK
    pmax = pair_slot.shape[1]
    cap = requests.shape[1]
    phalf = pmax // pair_count.shape[1]
    half = features // n_rep
    per_dev = pmax // (n_layer * n_rep)
    rep_index = lax.axis_index("rep")
    span_index = lax.axis_index("span")
    rows = BLOCK // ROW_CHUNKS
    lh = l_dev * half

    q5 = queries.reshape(n_query // BLOCK, BLOCK, l_dev, n_rep, half)
    p_half = lax.dynamic_index_in_dim(
        precond.reshape(l_dev, n_rep, half), rep_index, axis=1, keepdims=False
    ).reshape(lh)
    train = train_grads.reshape(tb_dev * BLOCK, l_dev, n_span, n_rep, half)
    train = lax.dynamic_index_in_dim(train, rep_index, axis=3, keepdims=False)
    train = jnp.transpose(train, (0, 2, 1, 3)).reshape(tb_dev * BLOCK, n_span, lh)
    sources = (span_index - jnp.arange(n_span, dtype=jnp.int32) + n_span) % n_span
    train = jnp.take(train, sources, axis=1)
    train = jnp.concatenate([train, jnp.zeros((BLOCK, n_span, lh), train.dtype)], axis=0)

    score_scale = 1.0 / math.sqrt(l_dev * n_layer * d_full)
    slot_row = pair_slot[0]
    train_row = pair_train[0]
    counts = pair_count[0]
    slots = jnp.arange(pmax, dtype=jnp.int32)
    live = (slots % phalf) < counts[slots // phalf]
    pick_train = jnp.where(live, train_row, tb_dev)

    def prepared_piece(dest, chunk):
        req_row = requests[dest]
        got = q5[req_row, chunk * rows:(chunk + 1) * rows, :, rep_index, :]
        got = (got.reshape(cap, rows, lh).astype(jnp.float32) * p_half).astype(jnp.bfloat16)
        return got

    outs = []
    for chunk in range(ROW_CHUNKS):
        pieces = [prepared_piece(span_index, chunk)]
        for k in range(1, n_span):
            dest = (span_index + k) % n_span
            perm = [(i, (i + k) % n_span) for i in range(n_span)]
            pieces.append(lax.ppermute(prepared_piece(dest, chunk), "span", perm))
        arrived = jnp.stack(pieces, axis=0)
        combos = lax.dot_general(
            arrived,
            train,
            (((0, 3), (1, 2)), ((), ())),
            preferred_element_type=jnp.float32,
        ).reshape(cap, rows, tb_dev + 1, BLOCK)
        partial = combos.at[slot_row, :, pick_train, :].get(mode="promise_in_bounds") * score_scale
        partial = partial.reshape(n_layer, n_rep, per_dev, rows, BLOCK)
        partial = ring_reduce_scatter(partial, "rep", 1)
        partial = ring_reduce_scatter(partial, "layer", 0)
        outs.append(partial)
    summed = jnp.concatenate(outs, axis=1).reshape(per_dev * BLOCK, BLOCK)
    return summed[None]


def solution(mesh):
    placed = (
        P("groups", "layer", "span"),
        P(("groups", "span"), "layer", None),
        P("layer", "span"),
        P("groups", None),
        P(("groups", "span"), None),
        P(("groups", "span"), None),
        P(("groups", "span"), None),
    )
    return jax.shard_map(
        shards,
        mesh=mesh,
        in_specs=placed,
        out_specs=P(("groups", "span"), ("layer", "rep"), None),
        check_vma=False,
    )
```

```python
import math

import jax
import jax.numpy as jnp
from jax import lax
from jax.sharding import PartitionSpec as P

BLOCK = 128
ROW_CHUNKS = 2


def ring_reduce_scatter(x, axis_name, dim):
    n = lax.axis_size(axis_name)
    me = lax.axis_index(axis_name)

    def piece(c):
        return lax.dynamic_index_in_dim(x, c % n, axis=dim, keepdims=False)

    if n == 1:
        return piece(me)
    perm = [(i, (i + 1) % n) for i in range(n)]
    acc = piece(me - 1 + n)
    for t in range(n - 1):
        recv = lax.ppermute(acc, axis_name, perm)
        acc = recv + piece(me - 2 - t + 2 * n)
    return acc


def shards(queries, train_grads, precond, requests, pair_slot, pair_train, pair_count):
    n_query, l_dev, features = queries.shape
    n_span = lax.axis_size("span")
    n_rep = lax.axis_size("rep")
    n_layer = lax.axis_size("layer")
    n_train, _, d_full = train_grads.shape
    tb_dev = n_train // BLOCK
    pmax = pair_slot.shape[1]
    cap = requests.shape[1]
    phalf = pmax // pair_count.shape[1]
    half = features // n_rep
    per_dev = pmax // (n_layer * n_rep)
    rep_index = lax.axis_index("rep")
    span_index = lax.axis_index("span")
    rows = BLOCK // ROW_CHUNKS

    dests = (span_index + jnp.arange(n_span, dtype=jnp.int32)) % n_span
    sources = (span_index - jnp.arange(n_span, dtype=jnp.int32) + n_span) % n_span
    q_half = []
    t_half = []
    for layer in range(l_dev):
        q_l = lax.dynamic_slice_in_dim(queries[:, layer, :], rep_index * half, half, axis=1)
        q_l = q_l * 1
        q_half.append(q_l)
        t_l = train_grads[:, layer, :]
        for k in range(n_span):
            t_half.append(lax.dynamic_slice_in_dim(t_l, sources[k] * features + rep_index * half, half, axis=1))
    p_half = lax.dynamic_slice_in_dim(precond, rep_index * half, half, axis=1)
    train = jnp.concatenate(t_half, axis=1)
    train = jnp.concatenate([train, jnp.zeros((BLOCK, train.shape[1]), train.dtype)], axis=0)

    score_scale = 1.0 / math.sqrt(l_dev * n_layer * d_full)
    slot_row = pair_slot[0]
    train_row = pair_train[0]
    counts = pair_count[0]
    slots = jnp.arange(pmax, dtype=jnp.int32)
    live = (slots % phalf) < counts[slots // phalf]
    pick_train = jnp.where(live, train_row, tb_dev)
    row_in_block = jnp.arange(rows, dtype=jnp.int32)

    outs = []
    gate = None
    for chunk in range(ROW_CHUNKS):
        row_ids = requests[dests] * BLOCK + chunk * rows
        row_ids = row_ids[:, :, None] + row_in_block
        sent = []
        for layer in range(l_dev):
            got = q_half[layer][row_ids]
            sent.append((got.astype(jnp.float32) * p_half[layer]).astype(jnp.bfloat16))
        if gate is not None:
            sent, _ = lax.optimization_barrier((sent, gate))
        pieces = []
        for layer in range(l_dev):
            for k in range(n_span):
                piece = sent[layer][k]
                if k:
                    perm = [(i, (i + k) % n_span) for i in range(n_span)]
                    piece = lax.ppermute(piece, "span", perm)
                pieces.append(piece)
        gate = pieces
        arrived = jnp.concatenate(pieces, axis=-1).reshape(cap * rows, -1)
        combos = lax.dot_general(
            arrived,
            train,
            (((1,), (1,)), ((), ())),
            preferred_element_type=jnp.float32,
        ).reshape(cap, rows, tb_dev + 1, BLOCK)
        partial = combos.at[slot_row, :, pick_train, :].get(mode="promise_in_bounds") * score_scale
        partial = partial.reshape(n_layer, n_rep, per_dev, rows, BLOCK)
        partial = ring_reduce_scatter(partial, "rep", 1)
        partial = ring_reduce_scatter(partial, "layer", 0)
        outs.append(partial)
    summed = jnp.concatenate(outs, axis=1).reshape(per_dev * BLOCK, BLOCK)
    return summed[None]


def solution(mesh):
    placed = (
        P("groups", "layer", "span"),
        P(("groups", "span"), "layer", None),
        P("layer", "span"),
        P("groups", None),
        P(("groups", "span"), None),
        P(("groups", "span"), None),
        P(("groups", "span"), None),
    )
    return jax.shard_map(
        shards,
        mesh=mesh,
        in_specs=placed,
        out_specs=P(("groups", "span"), ("layer", "rep"), None),
        check_vma=False,
    )
```

```python
import math

import jax
import jax.numpy as jnp
from jax import lax
from jax.sharding import PartitionSpec as P


BLOCK = 128
ROW_CHUNKS = 2


def ring_reduce_scatter(x, axis_name, dim):
    n = lax.axis_size(axis_name)
    me = lax.axis_index(axis_name)

    def piece(c):
        return lax.dynamic_index_in_dim(x, c % n, axis=dim, keepdims=False)

    if n == 1:
        return piece(me)
    perm = [(i, (i + 1) % n) for i in range(n)]
    acc = piece(me - 1 + n)
    for t in range(n - 1):
        recv = lax.ppermute(acc, axis_name, perm)
        acc = recv + piece(me - 2 - t + 2 * n)
    return acc


def shards(queries, train_grads, precond, requests, pair_slot, pair_train, pair_count):
    _, l_dev, features = queries.shape
    n_span = lax.axis_size("span")
    n_rep = lax.axis_size("rep")
    n_layer = lax.axis_size("layer")
    n_train, _, d_full = train_grads.shape
    tb_dev = n_train // BLOCK
    pmax = pair_slot.shape[1]
    cap = requests.shape[1]
    phalf = pmax // pair_count.shape[1]
    half = features // n_rep
    per_dev = pmax // (n_layer * n_rep)
    rep_index = lax.axis_index("rep")
    span_index = lax.axis_index("span")
    rows = BLOCK // ROW_CHUNKS

    dests = (span_index + jnp.arange(n_span, dtype=jnp.int32)) % n_span
    sources = (span_index - jnp.arange(n_span, dtype=jnp.int32) + n_span) % n_span
    q_half = []
    t_half = []
    for layer in range(l_dev):
        q_l = lax.dynamic_slice_in_dim(queries[:, layer, :], rep_index * half, half, axis=1)
        q_l = q_l * 1
        q_half.append(q_l)
        t_l = train_grads[:, layer, :]
        for k in range(n_span):
            t_half.append(lax.dynamic_slice_in_dim(t_l, sources[k] * features + rep_index * half, half, axis=1))
    p_half = lax.dynamic_slice_in_dim(precond, rep_index * half, half, axis=1)
    train = jnp.concatenate(t_half, axis=1)
    train = jnp.concatenate([train, jnp.zeros((BLOCK, train.shape[1]), train.dtype)], axis=0)

    score_scale = 1.0 / math.sqrt(l_dev * n_layer * d_full)
    slot_row = pair_slot[0]
    train_row = pair_train[0]
    counts = pair_count[0]
    slots = jnp.arange(pmax, dtype=jnp.int32)
    live = (slots % phalf) < counts[slots // phalf]
    pick_train = jnp.where(live, train_row, tb_dev)
    row_in_block = jnp.arange(rows, dtype=jnp.int32)

    outs = []
    gate = None
    for chunk in range(ROW_CHUNKS):
        row_ids = requests[dests] * BLOCK + chunk * rows
        row_ids = row_ids[:, :, None] + row_in_block
        if gate is not None:
            row_ids, _ = lax.optimization_barrier((row_ids, prev_sent))
        sent = []
        for layer in range(l_dev):
            got = q_half[layer][row_ids]
            sent.append((got.astype(jnp.float32) * p_half[layer]).astype(jnp.bfloat16))
        prev_sent = sent
        if gate is not None:
            sent, _ = lax.optimization_barrier((sent, gate))
        pieces = []
        for layer in range(l_dev):
            for k in range(n_span):
                piece = sent[layer][k]
                if k:
                    perm = [(i, (i + k) % n_span) for i in range(n_span)]
                    piece = lax.ppermute(piece, "span", perm)
                pieces.append(piece)
        gate = pieces
        arrived = jnp.concatenate(pieces, axis=-1).reshape(cap * rows, -1)
        combos = lax.dot_general(
            arrived,
            train,
            (((1,), (1,)), ((), ())),
            preferred_element_type=jnp.float32,
        ).reshape(cap, rows, tb_dev + 1, BLOCK)
        partial = combos.at[slot_row, :, pick_train, :].get(mode="promise_in_bounds") * score_scale
        partial = partial.reshape(n_layer, n_rep, per_dev, rows, BLOCK)
        partial = ring_reduce_scatter(partial, "rep", 1)
        partial = ring_reduce_scatter(partial, "layer", 0)
        outs.append(partial)
    summed = jnp.concatenate(outs, axis=1).reshape(per_dev * BLOCK, BLOCK)
    return summed[None]


def solution(mesh):
    placed = (
        P("groups", "layer", "span"),
        P(("groups", "span"), "layer", None),
        P("layer", "span"),
        P("groups", None),
        P(("groups", "span"), None),
        P(("groups", "span"), None),
        P(("groups", "span"), None),
    )

    return jax.shard_map(
        shards,
        mesh=mesh,
        in_specs=placed,
        out_specs=P(("groups", "span"), ("layer", "rep"), None),
        check_vma=False,
    )
```

```python
import math

import jax
import jax.numpy as jnp
from jax import lax
from jax.sharding import PartitionSpec as P


BLOCK = 128
ROW_SPLIT = (80, 48)


def ring_reduce_scatter(x, axis_name, dim):
    n = lax.axis_size(axis_name)
    me = lax.axis_index(axis_name)

    def piece(c):
        return lax.dynamic_index_in_dim(x, c % n, axis=dim, keepdims=False)

    if n == 1:
        return piece(me)
    perm = [(i, (i + 1) % n) for i in range(n)]
    acc = piece(me - 1 + n)
    for t in range(n - 1):
        recv = lax.ppermute(acc, axis_name, perm)
        acc = recv + piece(me - 2 - t + 2 * n)
    return acc


def shards(queries, train_grads, precond, requests, pair_slot, pair_train, pair_count):
    _, l_dev, features = queries.shape
    n_span = lax.axis_size("span")
    n_rep = lax.axis_size("rep")
    n_layer = lax.axis_size("layer")
    n_train, _, d_full = train_grads.shape
    tb_dev = n_train // BLOCK
    pmax = pair_slot.shape[1]
    cap = requests.shape[1]
    phalf = pmax // pair_count.shape[1]
    half = features // n_rep
    per_dev = pmax // (n_layer * n_rep)
    rep_index = lax.axis_index("rep")
    span_index = lax.axis_index("span")

    dests = (span_index + jnp.arange(n_span, dtype=jnp.int32)) % n_span
    sources = (span_index - jnp.arange(n_span, dtype=jnp.int32) + n_span) % n_span
    q_half = []
    t_half = []
    for layer in range(l_dev):
        q_l = lax.dynamic_slice_in_dim(queries[:, layer, :], rep_index * half, half, axis=1)
        q_l = q_l * 1
        q_half.append(q_l)
        t_l = train_grads[:, layer, :]
        for k in range(n_span):
            t_half.append(lax.dynamic_slice_in_dim(t_l, sources[k] * features + rep_index * half, half, axis=1))
    p_half = lax.dynamic_slice_in_dim(precond, rep_index * half, half, axis=1)
    train = jnp.concatenate(t_half, axis=1)
    train = jnp.concatenate([train, jnp.zeros((BLOCK, train.shape[1]), train.dtype)], axis=0)

    score_scale = 1.0 / math.sqrt(l_dev * n_layer * d_full)
    slot_row = pair_slot[0]
    train_row = pair_train[0]
    counts = pair_count[0]
    slots = jnp.arange(pmax, dtype=jnp.int32)
    live = (slots % phalf) < counts[slots // phalf]
    pick_train = jnp.where(live, train_row, tb_dev)

    outs = []
    gate = None
    row_start = 0
    for rows in ROW_SPLIT:
        row_ids = requests[dests] * BLOCK + row_start
        row_ids = row_ids[:, :, None] + jnp.arange(rows, dtype=jnp.int32)
        row_start += rows
        if gate is not None:
            row_ids, _ = lax.optimization_barrier((row_ids, prev_sent))
        sent = []
        for layer in range(l_dev):
            got = q_half[layer][row_ids]
            sent.append((got.astype(jnp.float32) * p_half[layer]).astype(jnp.bfloat16))
        prev_sent = sent
        if gate is not None:
            sent, _ = lax.optimization_barrier((sent, gate))
        pieces = []
        for layer in range(l_dev):
            for k in range(n_span):
                piece = sent[layer][k]
                if k:
                    perm = [(i, (i + k) % n_span) for i in range(n_span)]
                    piece = lax.ppermute(piece, "span", perm)
                pieces.append(piece)
        gate = pieces
        arrived = jnp.concatenate(pieces, axis=-1).reshape(cap * rows, -1)
        combos = lax.dot_general(
            arrived,
            train,
            (((1,), (1,)), ((), ())),
            preferred_element_type=jnp.float32,
        ).reshape(cap, rows, tb_dev + 1, BLOCK)
        partial = combos.at[slot_row, :, pick_train, :].get(mode="promise_in_bounds") * score_scale
        partial = partial.reshape(n_layer, n_rep, per_dev, rows, BLOCK)
        partial = ring_reduce_scatter(partial, "rep", 1)
        partial = ring_reduce_scatter(partial, "layer", 0)
        outs.append(partial)
    summed = jnp.concatenate(outs, axis=1).reshape(per_dev * BLOCK, BLOCK)
    return summed[None]


def solution(mesh):
    placed = (
        P("groups", "layer", "span"),
        P(("groups", "span"), "layer", None),
        P("layer", "span"),
        P("groups", None),
        P(("groups", "span"), None),
        P(("groups", "span"), None),
        P(("groups", "span"), None),
    )

    return jax.shard_map(
        shards,
        mesh=mesh,
        in_specs=placed,
        out_specs=P(("groups", "span"), ("layer", "rep"), None),
        check_vma=False,
    )
```

```python
import math

import jax
import jax.numpy as jnp
from jax import lax
from jax.sharding import PartitionSpec as P


BLOCK = 128
ROW_SPLIT = (80, 48)


def ring_reduce_scatter(x, axis_name, dim):
    n = lax.axis_size(axis_name)
    me = lax.axis_index(axis_name)

    def piece(c):
        return lax.dynamic_index_in_dim(x, c % n, axis=dim, keepdims=False)

    if n == 1:
        return piece(me)
    perm = [(i, (i + 1) % n) for i in range(n)]
    acc = piece(me - 1 + n)
    for t in range(n - 1):
        recv = lax.ppermute(acc, axis_name, perm)
        acc = recv + piece(me - 2 - t + 2 * n)
    return acc


def shards(queries, train_grads, precond, requests, pair_slot, pair_train, pair_count):
    n_query, l_dev, features = queries.shape
    n_span = lax.axis_size("span")
    n_rep = lax.axis_size("rep")
    n_layer = lax.axis_size("layer")
    n_train, _, d_full = train_grads.shape
    tb_dev = n_train // BLOCK
    pmax = pair_slot.shape[1]
    cap = requests.shape[1]
    phalf = pmax // pair_count.shape[1]
    half = features // n_rep
    per_dev = pmax // (n_layer * n_rep)
    rep_index = lax.axis_index("rep")
    span_index = lax.axis_index("span")

    dests = (span_index + jnp.arange(n_span, dtype=jnp.int32)) % n_span
    sources = (span_index - jnp.arange(n_span, dtype=jnp.int32) + n_span) % n_span
    q_half = []
    t_half = []
    for layer in range(l_dev):
        q_l = lax.dynamic_slice_in_dim(queries[:, layer, :], rep_index * half, half, axis=1)
        q_l = q_l * 1
        q_half.append(q_l)
        t_l = train_grads[:, layer, :]
        for k in range(n_span):
            t_half.append(lax.dynamic_slice_in_dim(t_l, sources[k] * features + rep_index * half, half, axis=1))
    p_half = lax.dynamic_slice_in_dim(precond, rep_index * half, half, axis=1)
    train = jnp.concatenate(t_half, axis=1)
    train = jnp.concatenate([train, jnp.zeros((BLOCK, train.shape[1]), train.dtype)], axis=0)

    score_scale = 1.0 / math.sqrt(l_dev * n_layer * d_full)
    slot_row = pair_slot[0]
    train_row = pair_train[0]
    counts = pair_count[0]
    slots = jnp.arange(pmax, dtype=jnp.int32)
    live = (slots % phalf) < counts[slots // phalf]
    pick_train = jnp.where(live, train_row, tb_dev)

    outs = []
    gate = None
    row_start = 0
    for rows in ROW_SPLIT:
        block_ids = requests[dests].reshape(-1)
        if gate is not None:
            block_ids, _ = lax.optimization_barrier((block_ids, prev_sent))
        sent = []
        for layer in range(l_dev):
            q3 = q_half[layer].reshape(n_query // BLOCK, BLOCK, half)
            got = jnp.take(q3[:, row_start:row_start + rows], block_ids, axis=0)
            got = got.reshape(n_span, cap, rows, half)
            sent.append((got.astype(jnp.float32) * p_half[layer]).astype(jnp.bfloat16))
        row_start += rows
        prev_sent = sent
        if gate is not None:
            sent, _ = lax.optimization_barrier((sent, gate))
        pieces = []
        for layer in range(l_dev):
            for k in range(n_span):
                piece = sent[layer][k]
                if k:
                    perm = [(i, (i + k) % n_span) for i in range(n_span)]
                    piece = lax.ppermute(piece, "span", perm)
                pieces.append(piece)
        gate = pieces
        arrived = jnp.concatenate(pieces, axis=-1).reshape(cap * rows, -1)
        combos = lax.dot_general(
            arrived,
            train,
            (((1,), (1,)), ((), ())),
            preferred_element_type=jnp.float32,
        ).reshape(cap, rows, tb_dev + 1, BLOCK)
        partial = combos.at[slot_row, :, pick_train, :].get(mode="promise_in_bounds") * score_scale
        partial = partial.reshape(n_layer, n_rep, per_dev, rows, BLOCK)
        partial = ring_reduce_scatter(partial, "rep", 1)
        partial = ring_reduce_scatter(partial, "layer", 0)
        outs.append(partial)
    summed = jnp.concatenate(outs, axis=1).reshape(per_dev * BLOCK, BLOCK)
    return summed[None]


def solution(mesh):
    placed = (
        P("groups", "layer", "span"),
        P(("groups", "span"), "layer", None),
        P("layer", "span"),
        P("groups", None),
        P(("groups", "span"), None),
        P(("groups", "span"), None),
        P(("groups", "span"), None),
    )

    return jax.shard_map(
        shards,
        mesh=mesh,
        in_specs=placed,
        out_specs=P(("groups", "span"), ("layer", "rep"), None),
        check_vma=False,
    )
```

```python
import math

import jax
import jax.numpy as jnp
from jax import lax
from jax.sharding import PartitionSpec as P


BLOCK = 128
ROW_SPLIT = (96, 32)
GATE = True


def ring_reduce_scatter(x, axis_name, dim):
    n = lax.axis_size(axis_name)
    me = lax.axis_index(axis_name)

    def piece(c):
        return lax.dynamic_index_in_dim(x, c % n, axis=dim, keepdims=False)

    if n == 1:
        return piece(me)
    perm = [(i, (i + 1) % n) for i in range(n)]
    acc = piece(me - 1 + n)
    for t in range(n - 1):
        recv = lax.ppermute(acc, axis_name, perm)
        acc = recv + piece(me - 2 - t + 2 * n)
    return acc


def shards(queries, train_grads, precond, requests, pair_slot, pair_train, pair_count):
    n_query, l_dev, features = queries.shape
    n_span = lax.axis_size("span")
    n_rep = lax.axis_size("rep")
    n_layer = lax.axis_size("layer")
    n_train, _, d_full = train_grads.shape
    tb_dev = n_train // BLOCK
    pmax = pair_slot.shape[1]
    cap = requests.shape[1]
    phalf = pmax // pair_count.shape[1]
    half = features // n_rep
    per_dev = pmax // (n_layer * n_rep)
    rep_index = lax.axis_index("rep")
    span_index = lax.axis_index("span")

    dests = (span_index + jnp.arange(n_span, dtype=jnp.int32)) % n_span
    sources = (span_index - jnp.arange(n_span, dtype=jnp.int32) + n_span) % n_span
    q_half = []
    t_half = []
    for layer in range(l_dev):
        q_l = lax.dynamic_slice_in_dim(queries[:, layer, :], rep_index * half, half, axis=1)
        q_l = q_l * 1
        q_half.append(q_l)
        t_l = train_grads[:, layer, :]
        for k in range(n_span):
            t_half.append(lax.dynamic_slice_in_dim(t_l, sources[k] * features + rep_index * half, half, axis=1))
    p_half = lax.dynamic_slice_in_dim(precond, rep_index * half, half, axis=1)
    train = jnp.concatenate(t_half, axis=1)
    train = jnp.concatenate([train, jnp.zeros((BLOCK, train.shape[1]), train.dtype)], axis=0)

    score_scale = 1.0 / math.sqrt(l_dev * n_layer * d_full)
    slot_row = pair_slot[0]
    train_row = pair_train[0]
    counts = pair_count[0]
    slots = jnp.arange(pmax, dtype=jnp.int32)
    live = (slots % phalf) < counts[slots // phalf]
    pick_train = jnp.where(live, train_row, tb_dev)

    outs = []
    gate = None
    row_start = 0
    for rows in ROW_SPLIT:
        block_ids = requests[dests].reshape(-1)
        if gate is not None:
            block_ids, _ = lax.optimization_barrier((block_ids, prev_sent))
        sent = []
        for layer in range(l_dev):
            q3 = q_half[layer].reshape(n_query // BLOCK, BLOCK, half)
            got = jnp.take(q3[:, row_start:row_start + rows], block_ids, axis=0)
            got = got.reshape(n_span, cap, rows, half)
            sent.append((got.astype(jnp.float32) * p_half[layer]).astype(jnp.bfloat16))
        row_start += rows
        prev_sent = sent
        if GATE and gate is not None:
            sent, _ = lax.optimization_barrier((sent, gate))
        pieces = []
        for layer in range(l_dev):
            for k in range(n_span):
                piece = sent[layer][k]
                if k:
                    perm = [(i, (i + k) % n_span) for i in range(n_span)]
                    piece = lax.ppermute(piece, "span", perm)
                pieces.append(piece)
        gate = pieces
        arrived = jnp.concatenate(pieces, axis=-1).reshape(cap * rows, -1)
        combos = lax.dot_general(
            arrived,
            train,
            (((1,), (1,)), ((), ())),
            preferred_element_type=jnp.float32,
        ).reshape(cap, rows, tb_dev + 1, BLOCK)
        partial = combos.at[slot_row, :, pick_train, :].get(mode="promise_in_bounds") * score_scale
        partial = partial.reshape(n_layer, n_rep, per_dev, rows, BLOCK)
        partial = ring_reduce_scatter(partial, "rep", 1)
        partial = ring_reduce_scatter(partial, "layer", 0)
        outs.append(partial)
    summed = jnp.concatenate(outs, axis=1).reshape(per_dev * BLOCK, BLOCK)
    return summed[None]


def solution(mesh):
    placed = (
        P("groups", "layer", "span"),
        P(("groups", "span"), "layer", None),
        P("layer", "span"),
        P("groups", None),
        P(("groups", "span"), None),
        P(("groups", "span"), None),
        P(("groups", "span"), None),
    )

    return jax.shard_map(
        shards,
        mesh=mesh,
        in_specs=placed,
        out_specs=P(("groups", "span"), ("layer", "rep"), None),
        check_vma=False,
    )
```

```python
import math

import jax
import jax.numpy as jnp
from jax import lax
from jax.sharding import PartitionSpec as P


BLOCK = 128
ROW_SPLIT = (24, 40)
GATE = False


def ring_reduce_scatter(x, axis_name, dim):
    n = lax.axis_size(axis_name)
    me = lax.axis_index(axis_name)

    def piece(c):
        return lax.dynamic_index_in_dim(x, c % n, axis=dim, keepdims=False)

    if n == 1:
        return piece(me)
    perm = [(i, (i + 1) % n) for i in range(n)]
    acc = piece(me - 1 + n)
    for t in range(n - 1):
        recv = lax.ppermute(acc, axis_name, perm)
        acc = recv + piece(me - 2 - t + 2 * n)
    return acc


def shards(queries, train_grads, precond, requests, pair_slot, pair_train, pair_count):
    n_query, l_dev, features = queries.shape
    n_span = lax.axis_size("span")
    n_rep = lax.axis_size("rep")
    n_layer = lax.axis_size("layer")
    n_train, _, d_full = train_grads.shape
    tb_dev = n_train // BLOCK
    pmax = pair_slot.shape[1]
    cap = requests.shape[1]
    phalf = pmax // pair_count.shape[1]
    per_dev = pmax // (n_layer * n_rep)
    rep_index = lax.axis_index("rep")
    span_index = lax.axis_index("span")
    own_rows = BLOCK // n_rep

    dests = (span_index + jnp.arange(n_span, dtype=jnp.int32)) % n_span
    sources = (span_index - jnp.arange(n_span, dtype=jnp.int32) + n_span) % n_span
    t_parts = []
    for layer in range(l_dev):
        t_l = train_grads[:, layer, :]
        for k in range(n_span):
            t_parts.append(lax.dynamic_slice_in_dim(t_l, sources[k] * features, features, axis=1))
    train = jnp.concatenate(t_parts, axis=1)
    train = jnp.concatenate([train, jnp.zeros((BLOCK, train.shape[1]), train.dtype)], axis=0)

    score_scale = 1.0 / math.sqrt(l_dev * n_layer * d_full)
    slot_row = pair_slot[0]
    train_row = pair_train[0]
    counts = pair_count[0]
    slots = jnp.arange(pmax, dtype=jnp.int32)
    live = (slots % phalf) < counts[slots // phalf]
    pick_train = jnp.where(live, train_row, tb_dev)

    outs = []
    gate = None
    row_start = 0
    for rows in ROW_SPLIT:
        block_ids = requests[dests].reshape(-1)
        if gate is not None:
            block_ids, _ = lax.optimization_barrier((block_ids, prev_sent))
        sent = []
        for layer in range(l_dev):
            q3 = queries[:, layer, :].reshape(n_query // BLOCK, BLOCK, features)
            q3 = lax.dynamic_slice_in_dim(q3, rep_index * own_rows + row_start, rows, axis=1)
            got = jnp.take(q3, block_ids, axis=0).reshape(n_span, cap, rows, features)
            sent.append((got.astype(jnp.float32) * precond[layer]).astype(jnp.bfloat16))
        row_start += rows
        prev_sent = sent
        if GATE and gate is not None:
            sent, _ = lax.optimization_barrier((sent, gate))
        pieces = []
        for layer in range(l_dev):
            for k in range(n_span):
                piece = sent[layer][k]
                if k:
                    perm = [(i, (i + k) % n_span) for i in range(n_span)]
                    piece = lax.ppermute(piece, "span", perm)
                pieces.append(piece)
        gate = pieces
        arrived = jnp.concatenate(pieces, axis=-1).reshape(cap * rows, -1)
        combos = lax.dot_general(
            arrived,
            train,
            (((1,), (1,)), ((), ())),
            preferred_element_type=jnp.float32,
        ).reshape(cap, rows, tb_dev + 1, BLOCK)
        partial = combos.at[slot_row, :, pick_train, :].get(mode="promise_in_bounds") * score_scale
        partial = partial.reshape(n_layer, n_rep, per_dev, rows, BLOCK)
        partial = ring_reduce_scatter(partial, "layer", 0)
        got_rows = [lax.dynamic_index_in_dim(partial, rep_index, axis=0, keepdims=False)]
        for k in range(1, n_rep):
            perm = [(i, (i + k) % n_rep) for i in range(n_rep)]
            send = lax.dynamic_index_in_dim(partial, (rep_index + k) % n_rep, axis=0, keepdims=False)
            got_rows.append(lax.ppermute(send, "rep", perm))
        by_owner = jnp.stack(got_rows, axis=0)
        owner_order = (rep_index - jnp.arange(n_rep, dtype=jnp.int32) + n_rep) % n_rep
        order = jnp.argsort(owner_order)
        by_owner = jnp.take(by_owner, order, axis=0)
        outs.append(by_owner)
    summed = jnp.concatenate(outs, axis=2)
    summed = jnp.transpose(summed, (1, 0, 2, 3)).reshape(per_dev * BLOCK, BLOCK)
    return summed[None]


def solution(mesh):
    placed = (
        P("groups", "layer", "span"),
        P(("groups", "span"), "layer", None),
        P("layer", "span"),
        P("groups", None),
        P(("groups", "span"), None),
        P(("groups", "span"), None),
        P(("groups", "span"), None),
    )

    return jax.shard_map(
        shards,
        mesh=mesh,
        in_specs=placed,
        out_specs=P(("groups", "span"), ("layer", "rep"), None),
        check_vma=False,
    )
```

```python
import math

import jax
import jax.numpy as jnp
from jax import lax
from jax.sharding import PartitionSpec as P


BLOCK = 128
ROW_SPLIT = (24, 40)
GATE = False


def ring_reduce_scatter(x, axis_name, dim):
    n = lax.axis_size(axis_name)
    me = lax.axis_index(axis_name)

    def piece(c):
        return lax.dynamic_index_in_dim(x, c % n, axis=dim, keepdims=False)

    if n == 1:
        return piece(me)
    perm = [(i, (i + 1) % n) for i in range(n)]
    acc = piece(me - 1 + n)
    for t in range(n - 1):
        recv = lax.ppermute(acc, axis_name, perm)
        acc = recv + piece(me - 2 - t + 2 * n)
    return acc


def shards(queries, train_grads, precond, requests, pair_slot, pair_train, pair_count):
    n_query, l_dev, features = queries.shape
    n_span = lax.axis_size("span")
    n_rep = lax.axis_size("rep")
    n_layer = lax.axis_size("layer")
    n_train, _, d_full = train_grads.shape
    tb_dev = n_train // BLOCK
    pmax = pair_slot.shape[1]
    cap = requests.shape[1]
    phalf = pmax // pair_count.shape[1]
    per_dev = pmax // (n_layer * n_rep)
    rep_index = lax.axis_index("rep")
    span_index = lax.axis_index("span")
    own_rows = BLOCK // n_rep

    dests = (span_index + jnp.arange(n_span, dtype=jnp.int32)) % n_span
    sources = (span_index - jnp.arange(n_span, dtype=jnp.int32) + n_span) % n_span
    t_parts = []
    for layer in range(l_dev):
        t_l = train_grads[:, layer, :]
        for k in range(n_span):
            t_parts.append(lax.dynamic_slice_in_dim(t_l, sources[k] * features, features, axis=1))
    train = jnp.concatenate(t_parts, axis=1)
    train = jnp.concatenate([train, jnp.zeros((BLOCK, train.shape[1]), train.dtype)], axis=0)

    score_scale = 1.0 / math.sqrt(l_dev * n_layer * d_full)
    slot_row = pair_slot[0]
    train_row = pair_train[0]
    counts = pair_count[0]
    slots = jnp.arange(pmax, dtype=jnp.int32)
    live = (slots % phalf) < counts[slots // phalf]
    pick_train = jnp.where(live, train_row, tb_dev)

    outs = []
    gate = None
    row_start = 0
    for rows in ROW_SPLIT:
        block_ids = requests[dests].reshape(-1)
        if gate is not None:
            block_ids, _ = lax.optimization_barrier((block_ids, prev_sent))
        sent = []
        for layer in range(l_dev):
            q3 = queries[:, layer, :].reshape(n_query // BLOCK, BLOCK, features)
            q3 = lax.dynamic_slice_in_dim(q3, rep_index * own_rows + row_start, rows, axis=1)
            got = jnp.take(q3, block_ids, axis=0).reshape(n_span, cap, rows, features)
            sent.append((got.astype(jnp.float32) * precond[layer]).astype(jnp.bfloat16))
        row_start += rows
        prev_sent = sent
        if GATE and gate is not None:
            sent, _ = lax.optimization_barrier((sent, gate))
        pieces = []
        for layer in range(l_dev):
            for k in range(n_span):
                piece = sent[layer][k]
                if k:
                    perm = [(i, (i + k) % n_span) for i in range(n_span)]
                    piece = lax.ppermute(piece, "span", perm)
                pieces.append(piece)
        gate = pieces
        dims = (((1,), (1,)), ((), ()))
        local = jnp.concatenate([pieces[layer * n_span] for layer in range(l_dev)], axis=-1)
        local_train = jnp.concatenate(
            [train[:, layer * n_span * features:(layer * n_span + 1) * features] for layer in range(l_dev)],
            axis=1,
        )
        combos = lax.dot_general(local.reshape(cap * rows, -1), local_train, dims, preferred_element_type=jnp.float32)
        remote = [p for i, p in enumerate(pieces) if i % n_span]
        remote_train = jnp.concatenate(
            [train[:, (layer * n_span + 1) * features:(layer + 1) * n_span * features] for layer in range(l_dev)],
            axis=1,
        )
        arrived = jnp.concatenate(remote, axis=-1).reshape(cap * rows, -1)
        combos = combos + lax.dot_general(arrived, remote_train, dims, preferred_element_type=jnp.float32)
        combos = combos.reshape(cap, rows, tb_dev + 1, BLOCK)
        partial = combos.at[slot_row, :, pick_train, :].get(mode="promise_in_bounds") * score_scale
        partial = partial.reshape(n_layer, n_rep, per_dev, rows, BLOCK)
        partial = ring_reduce_scatter(partial, "layer", 0)
        got_rows = [lax.dynamic_index_in_dim(partial, rep_index, axis=0, keepdims=False)]
        for k in range(1, n_rep):
            perm = [(i, (i + k) % n_rep) for i in range(n_rep)]
            send = lax.dynamic_index_in_dim(partial, (rep_index + k) % n_rep, axis=0, keepdims=False)
            got_rows.append(lax.ppermute(send, "rep", perm))
        by_owner = jnp.stack(got_rows, axis=0)
        owner_order = (rep_index - jnp.arange(n_rep, dtype=jnp.int32) + n_rep) % n_rep
        order = jnp.argsort(owner_order)
        by_owner = jnp.take(by_owner, order, axis=0)
        outs.append(by_owner)
    summed = jnp.concatenate(outs, axis=2)
    summed = jnp.transpose(summed, (1, 0, 2, 3)).reshape(per_dev * BLOCK, BLOCK)
    return summed[None]


def solution(mesh):
    placed = (
        P("groups", "layer", "span"),
        P(("groups", "span"), "layer", None),
        P("layer", "span"),
        P("groups", None),
        P(("groups", "span"), None),
        P(("groups", "span"), None),
        P(("groups", "span"), None),
    )

    return jax.shard_map(
        shards,
        mesh=mesh,
        in_specs=placed,
        out_specs=P(("groups", "span"), ("layer", "rep"), None),
        check_vma=False,
    )
```

```python
import math

import jax
import jax.numpy as jnp
from jax import lax
from jax.sharding import PartitionSpec as P


BLOCK = 128
ROW_SPLIT = (24, 32, 8)
GATE_FROM = {2: 0}


def ring_reduce_scatter(x, axis_name, dim):
    n = lax.axis_size(axis_name)
    me = lax.axis_index(axis_name)

    def piece(c):
        return lax.dynamic_index_in_dim(x, c % n, axis=dim, keepdims=False)

    if n == 1:
        return piece(me)
    perm = [(i, (i + 1) % n) for i in range(n)]
    acc = piece(me - 1 + n)
    for t in range(n - 1):
        recv = lax.ppermute(acc, axis_name, perm)
        acc = recv + piece(me - 2 - t + 2 * n)
    return acc


def shards(queries, train_grads, precond, requests, pair_slot, pair_train, pair_count):
    n_query, l_dev, features = queries.shape
    n_span = lax.axis_size("span")
    n_rep = lax.axis_size("rep")
    n_layer = lax.axis_size("layer")
    n_train, _, d_full = train_grads.shape
    tb_dev = n_train // BLOCK
    pmax = pair_slot.shape[1]
    cap = requests.shape[1]
    phalf = pmax // pair_count.shape[1]
    per_dev = pmax // (n_layer * n_rep)
    rep_index = lax.axis_index("rep")
    span_index = lax.axis_index("span")
    own_rows = BLOCK // n_rep

    dests = (span_index + jnp.arange(n_span, dtype=jnp.int32)) % n_span
    sources = (span_index - jnp.arange(n_span, dtype=jnp.int32) + n_span) % n_span
    t_parts = []
    for layer in range(l_dev):
        t_l = train_grads[:, layer, :]
        for k in range(n_span):
            t_parts.append(lax.dynamic_slice_in_dim(t_l, sources[k] * features, features, axis=1))
    train = jnp.concatenate(t_parts, axis=1)
    train = jnp.concatenate([train, jnp.zeros((BLOCK, train.shape[1]), train.dtype)], axis=0)

    score_scale = 1.0 / math.sqrt(l_dev * n_layer * d_full)
    slot_row = pair_slot[0]
    train_row = pair_train[0]
    counts = pair_count[0]
    slots = jnp.arange(pmax, dtype=jnp.int32)
    live = (slots % phalf) < counts[slots // phalf]
    pick_train = jnp.where(live, train_row, tb_dev)

    outs = []
    gate = None
    arrivals = []
    row_start = 0
    for chunk, rows in enumerate(ROW_SPLIT):
        block_ids = requests[dests].reshape(-1)
        if gate is not None:
            block_ids, _ = lax.optimization_barrier((block_ids, prev_sent))
        sent = []
        for layer in range(l_dev):
            q3 = queries[:, layer, :].reshape(n_query // BLOCK, BLOCK, features)
            q3 = lax.dynamic_slice_in_dim(q3, rep_index * own_rows + row_start, rows, axis=1)
            got = jnp.take(q3, block_ids, axis=0).reshape(n_span, cap, rows, features)
            sent.append((got.astype(jnp.float32) * precond[layer]).astype(jnp.bfloat16))
        row_start += rows
        prev_sent = sent
        if chunk in GATE_FROM:
            sent, _ = lax.optimization_barrier((sent, arrivals[GATE_FROM[chunk]]))
        pieces = []
        for layer in range(l_dev):
            for k in range(n_span):
                piece = sent[layer][k]
                if k:
                    perm = [(i, (i + k) % n_span) for i in range(n_span)]
                    piece = lax.ppermute(piece, "span", perm)
                pieces.append(piece)
        gate = pieces
        arrivals.append(pieces)
        arrived = jnp.concatenate(pieces, axis=-1).reshape(cap * rows, -1)
        combos = lax.dot_general(
            arrived,
            train,
            (((1,), (1,)), ((), ())),
            preferred_element_type=jnp.float32,
        ).reshape(cap, rows, tb_dev + 1, BLOCK)
        partial = combos.at[slot_row, :, pick_train, :].get(mode="promise_in_bounds") * score_scale
        partial = partial.reshape(n_layer, n_rep, per_dev, rows, BLOCK)
        partial = ring_reduce_scatter(partial, "layer", 0)
        got_rows = [lax.dynamic_index_in_dim(partial, rep_index, axis=0, keepdims=False)]
        for k in range(1, n_rep):
            perm = [(i, (i + k) % n_rep) for i in range(n_rep)]
            send = lax.dynamic_index_in_dim(partial, (rep_index + k) % n_rep, axis=0, keepdims=False)
            got_rows.append(lax.ppermute(send, "rep", perm))
        by_owner = jnp.stack(got_rows, axis=0)
        owner_order = (rep_index - jnp.arange(n_rep, dtype=jnp.int32) + n_rep) % n_rep
        order = jnp.argsort(owner_order)
        by_owner = jnp.take(by_owner, order, axis=0)
        outs.append(by_owner)
    summed = jnp.concatenate(outs, axis=2)
    summed = jnp.transpose(summed, (1, 0, 2, 3)).reshape(per_dev * BLOCK, BLOCK)
    return summed[None]


def solution(mesh):
    placed = (
        P("groups", "layer", "span"),
        P(("groups", "span"), "layer", None),
        P("layer", "span"),
        P("groups", None),
        P(("groups", "span"), None),
        P(("groups", "span"), None),
        P(("groups", "span"), None),
    )

    return jax.shard_map(
        shards,
        mesh=mesh,
        in_specs=placed,
        out_specs=P(("groups", "span"), ("layer", "rep"), None),
        check_vma=False,
    )
```

```python
import math

import jax
import jax.numpy as jnp
from jax import lax
from jax.sharding import PartitionSpec as P


BLOCK = 128
ROW_SPLIT = (8, 40, 16)
GATE_FROM = {2: 0}


def ring_reduce_scatter(x, axis_name, dim):
    n = lax.axis_size(axis_name)
    me = lax.axis_index(axis_name)

    def piece(c):
        return lax.dynamic_index_in_dim(x, c % n, axis=dim, keepdims=False)

    if n == 1:
        return piece(me)
    perm = [(i, (i + 1) % n) for i in range(n)]
    acc = piece(me - 1 + n)
    for t in range(n - 1):
        recv = lax.ppermute(acc, axis_name, perm)
        acc = recv + piece(me - 2 - t + 2 * n)
    return acc


def shards(queries, train_grads, precond, requests, pair_slot, pair_train, pair_count):
    n_query, l_dev, features = queries.shape
    n_span = lax.axis_size("span")
    n_rep = lax.axis_size("rep")
    n_layer = lax.axis_size("layer")
    n_train, _, d_full = train_grads.shape
    tb_dev = n_train // BLOCK
    pmax = pair_slot.shape[1]
    cap = requests.shape[1]
    phalf = pmax // pair_count.shape[1]
    per_dev = pmax // (n_layer * n_rep)
    rep_index = lax.axis_index("rep")
    span_index = lax.axis_index("span")
    own_rows = BLOCK // n_rep

    dests = (span_index + jnp.arange(n_span, dtype=jnp.int32)) % n_span
    sources = (span_index - jnp.arange(n_span, dtype=jnp.int32) + n_span) % n_span
    t_parts = []
    for layer in range(l_dev):
        t_l = train_grads[:, layer, :]
        for k in range(n_span):
            t_parts.append(lax.dynamic_slice_in_dim(t_l, sources[k] * features, features, axis=1))
    train = jnp.concatenate(t_parts, axis=1)

    score_scale = 1.0 / math.sqrt(l_dev * n_layer * d_full)
    slot_row = pair_slot[0]
    train_row = pair_train[0]
    counts = pair_count[0]
    slots = jnp.arange(pmax, dtype=jnp.int32)
    live = (slots % phalf) < counts[slots // phalf]

    outs = []
    gate = None
    arrivals = []
    row_start = 0
    for chunk, rows in enumerate(ROW_SPLIT):
        block_ids = requests[dests].reshape(-1)
        if gate is not None:
            block_ids, _ = lax.optimization_barrier((block_ids, prev_sent))
        sent = []
        for layer in range(l_dev):
            q3 = queries[:, layer, :].reshape(n_query // BLOCK, BLOCK, features)
            q3 = lax.dynamic_slice_in_dim(q3, rep_index * own_rows + row_start, rows, axis=1)
            got = jnp.take(q3, block_ids, axis=0, mode="clip").reshape(n_span, cap, rows, features)
            sent.append((got.astype(jnp.float32) * precond[layer]).astype(jnp.bfloat16))
        row_start += rows
        prev_sent = sent
        if chunk in GATE_FROM:
            sent, _ = lax.optimization_barrier((sent, arrivals[GATE_FROM[chunk]]))
        pieces = []
        for layer in range(l_dev):
            for k in range(n_span):
                piece = sent[layer][k]
                if k:
                    perm = [(i, (i + k) % n_span) for i in range(n_span)]
                    piece = lax.ppermute(piece, "span", perm)
                pieces.append(piece)
        gate = pieces
        arrivals.append(pieces)
        arrived = jnp.concatenate(pieces, axis=-1).reshape(cap * rows, -1)
        combos = lax.dot_general(
            arrived,
            train,
            (((1,), (1,)), ((), ())),
            preferred_element_type=jnp.float32,
        ).reshape(cap, rows, tb_dev, BLOCK)
        partial = combos.at[slot_row, :, train_row, :].get(mode="promise_in_bounds") * score_scale
        partial = jnp.where(live[:, None, None], partial, 0.0)
        partial = partial.reshape(n_layer, n_rep, per_dev, rows, BLOCK)
        partial = ring_reduce_scatter(partial, "layer", 0)
        got_rows = [lax.dynamic_index_in_dim(partial, rep_index, axis=0, keepdims=False)]
        for k in range(1, n_rep):
            perm = [(i, (i + k) % n_rep) for i in range(n_rep)]
            send = lax.dynamic_index_in_dim(partial, (rep_index + k) % n_rep, axis=0, keepdims=False)
            got_rows.append(lax.ppermute(send, "rep", perm))
        by_owner = jnp.stack(got_rows, axis=0)
        owner_order = (rep_index - jnp.arange(n_rep, dtype=jnp.int32) + n_rep) % n_rep
        order = jnp.argsort(owner_order)
        by_owner = jnp.take(by_owner, order, axis=0, mode="clip")
        outs.append(by_owner)
    summed = jnp.concatenate(outs, axis=2)
    summed = jnp.transpose(summed, (1, 0, 2, 3)).reshape(per_dev * BLOCK, BLOCK)
    return summed[None]


def solution(mesh):
    placed = (
        P("groups", "layer", "span"),
        P(("groups", "span"), "layer", None),
        P("layer", "span"),
        P("groups", None),
        P(("groups", "span"), None),
        P(("groups", "span"), None),
        P(("groups", "span"), None),
    )

    return jax.shard_map(
        shards,
        mesh=mesh,
        in_specs=placed,
        out_specs=P(("groups", "span"), ("layer", "rep"), None),
        check_vma=False,
    )
```

```python
import math

import jax
import jax.numpy as jnp
from jax import lax
from jax.sharding import PartitionSpec as P


BLOCK = 128
ROW_SPLIT = (8, 24, 32)
GATE_FROM = {2: 0}


def ring_reduce_scatter(x, axis_name, dim):
    n = lax.axis_size(axis_name)
    me = lax.axis_index(axis_name)

    def piece(c):
        return lax.dynamic_index_in_dim(x, c % n, axis=dim, keepdims=False)

    if n == 1:
        return piece(me)
    perm = [(i, (i + 1) % n) for i in range(n)]
    acc = piece(me - 1 + n)
    for t in range(n - 1):
        recv = lax.ppermute(acc, axis_name, perm)
        acc = recv + piece(me - 2 - t + 2 * n)
    return acc


def shards(queries, train_grads, precond, requests, pair_slot, pair_train, pair_count):
    n_query, l_dev, features = queries.shape
    n_span = lax.axis_size("span")
    n_rep = lax.axis_size("rep")
    n_layer = lax.axis_size("layer")
    n_train, _, d_full = train_grads.shape
    tb_dev = n_train // BLOCK
    pmax = pair_slot.shape[1]
    cap = requests.shape[1]
    phalf = pmax // pair_count.shape[1]
    per_dev = pmax // (n_layer * n_rep)
    rep_index = lax.axis_index("rep")
    span_index = lax.axis_index("span")
    own_rows = BLOCK // n_rep

    dests = (span_index + jnp.arange(n_span, dtype=jnp.int32)) % n_span
    sources = (span_index - jnp.arange(n_span, dtype=jnp.int32) + n_span) % n_span
    t_parts = []
    for layer in range(l_dev):
        t_l = train_grads[:, layer, :]
        for k in range(n_span):
            t_parts.append(lax.dynamic_slice_in_dim(t_l, sources[k] * features, features, axis=1))
    train = jnp.concatenate(t_parts, axis=1)
    train = jnp.concatenate([train, jnp.zeros((BLOCK, train.shape[1]), train.dtype)], axis=0)

    score_scale = 1.0 / math.sqrt(l_dev * n_layer * d_full)
    slot_row = pair_slot[0]
    train_row = pair_train[0]
    counts = pair_count[0]
    slots = jnp.arange(pmax, dtype=jnp.int32)
    live = (slots % phalf) < counts[slots // phalf]
    pick_train = jnp.where(live, train_row, tb_dev)

    out_buf = jnp.zeros((per_dev, BLOCK, BLOCK), jnp.float32)
    gate = None
    arrivals = []
    row_start = 0
    for chunk, rows in enumerate(ROW_SPLIT):
        block_ids = requests[dests].reshape(-1)
        if gate is not None:
            block_ids, _ = lax.optimization_barrier((block_ids, prev_sent))
        sent = []
        for layer in range(l_dev):
            q3 = queries[:, layer, :].reshape(n_query // BLOCK, BLOCK, features)
            q3 = lax.dynamic_slice_in_dim(q3, rep_index * own_rows + row_start, rows, axis=1)
            got = jnp.take(q3, block_ids, axis=0).reshape(n_span, cap, rows, features)
            sent.append((got.astype(jnp.float32) * precond[layer]).astype(jnp.bfloat16))
        row_start += rows
        prev_sent = sent
        if chunk in GATE_FROM:
            sent, _ = lax.optimization_barrier((sent, arrivals[GATE_FROM[chunk]]))
        pieces = []
        for layer in range(l_dev):
            for k in range(n_span):
                piece = sent[layer][k]
                if k:
                    perm = [(i, (i + k) % n_span) for i in range(n_span)]
                    piece = lax.ppermute(piece, "span", perm)
                pieces.append(piece)
        gate = pieces
        arrivals.append(pieces)
        arrived = jnp.concatenate(pieces, axis=-1).reshape(cap * rows, -1)
        combos = lax.dot_general(
            arrived,
            train,
            (((1,), (1,)), ((), ())),
            preferred_element_type=jnp.float32,
        ).reshape(cap, rows, tb_dev + 1, BLOCK)
        partial = combos.at[slot_row, :, pick_train, :].get(mode="promise_in_bounds") * score_scale
        partial = partial.reshape(n_layer, n_rep, per_dev, rows, BLOCK)
        partial = ring_reduce_scatter(partial, "layer", 0)
        got_rows = [lax.dynamic_index_in_dim(partial, rep_index, axis=0, keepdims=False)]
        for k in range(1, n_rep):
            perm = [(i, (i + k) % n_rep) for i in range(n_rep)]
            send = lax.dynamic_index_in_dim(partial, (rep_index + k) % n_rep, axis=0, keepdims=False)
            got_rows.append(lax.ppermute(send, "rep", perm))
        for k, got in enumerate(got_rows):
            owner = (rep_index - k + n_rep) % n_rep
            out_buf = lax.dynamic_update_slice(out_buf, got, (0, owner * own_rows + row_start - rows, 0))
    return out_buf.reshape(per_dev * BLOCK, BLOCK)[None]


def solution(mesh):
    placed = (
        P("groups", "layer", "span"),
        P(("groups", "span"), "layer", None),
        P("layer", "span"),
        P("groups", None),
        P(("groups", "span"), None),
        P(("groups", "span"), None),
        P(("groups", "span"), None),
    )

    return jax.shard_map(
        shards,
        mesh=mesh,
        in_specs=placed,
        out_specs=P(("groups", "span"), ("layer", "rep"), None),
        check_vma=False,
    )
```

```python
import math

import jax
import jax.numpy as jnp
from jax import lax
from jax.sharding import PartitionSpec as P


BLOCK = 128
ROW_SPLIT = (8, 24, 32)
GATE_FROM = {2: 0}


def ring_reduce_scatter(x, axis_name, dim):
    n = lax.axis_size(axis_name)
    me = lax.axis_index(axis_name)

    def piece(c):
        return lax.dynamic_index_in_dim(x, c % n, axis=dim, keepdims=False)

    if n == 1:
        return piece(me)
    perm = [(i, (i + 1) % n) for i in range(n)]
    acc = piece(me - 1 + n)
    for t in range(n - 1):
        recv = lax.ppermute(acc, axis_name, perm)
        acc = recv + piece(me - 2 - t + 2 * n)
    return acc


def shards(queries, train_grads, precond, requests, pair_slot, pair_train, pair_count):
    n_query, l_dev, features = queries.shape
    n_span = lax.axis_size("span")
    n_rep = lax.axis_size("rep")
    n_layer = lax.axis_size("layer")
    n_train, _, d_full = train_grads.shape
    tb_dev = n_train // BLOCK
    pmax = pair_slot.shape[1]
    cap = requests.shape[1]
    phalf = pmax // pair_count.shape[1]
    per_dev = pmax // (n_layer * n_rep)
    rep_index = lax.axis_index("rep")
    span_index = lax.axis_index("span")
    own_rows = BLOCK // n_rep

    dests = (span_index + jnp.arange(n_span, dtype=jnp.int32)) % n_span
    sources = (span_index - jnp.arange(n_span, dtype=jnp.int32) + n_span) % n_span
    t_parts = []
    for layer in range(l_dev):
        t_l = train_grads[:, layer, :]
        for k in range(n_span):
            t_parts.append(lax.dynamic_slice_in_dim(t_l, sources[k] * features, features, axis=1))
    train = jnp.concatenate(t_parts, axis=1)

    score_scale = 1.0 / math.sqrt(l_dev * n_layer * d_full)
    slot_row = pair_slot[0]
    train_row = pair_train[0]
    counts = pair_count[0]
    slots = jnp.arange(pmax, dtype=jnp.int32)
    live = (slots % phalf) < counts[slots // phalf]

    out_buf = jnp.zeros((per_dev, BLOCK, BLOCK), jnp.float32)
    gate = None
    arrivals = []
    row_start = 0
    for chunk, rows in enumerate(ROW_SPLIT):
        block_ids = requests[dests].reshape(-1)
        if gate is not None:
            block_ids, _ = lax.optimization_barrier((block_ids, prev_sent))
        sent = []
        for layer in range(l_dev):
            q3 = queries[:, layer, :].reshape(n_query // BLOCK, BLOCK, features)
            q3 = lax.dynamic_slice_in_dim(q3, rep_index * own_rows + row_start, rows, axis=1)
            got = jnp.take(q3, block_ids, axis=0, mode="clip").reshape(n_span, cap, rows, features)
            sent.append((got.astype(jnp.float32) * precond[layer]).astype(jnp.bfloat16))
        row_start += rows
        prev_sent = sent
        if chunk in GATE_FROM:
            sent, _ = lax.optimization_barrier((sent, arrivals[GATE_FROM[chunk]]))
        pieces = []
        for layer in range(l_dev):
            for k in range(n_span):
                piece = sent[layer][k]
                if k:
                    perm = [(i, (i + k) % n_span) for i in range(n_span)]
                    piece = lax.ppermute(piece, "span", perm)
                pieces.append(piece)
        gate = pieces
        arrivals.append(pieces)
        arrived = jnp.concatenate(pieces, axis=-1).reshape(cap * rows, -1)
        combos = lax.dot_general(
            arrived,
            train,
            (((1,), (1,)), ((), ())),
            preferred_element_type=jnp.float32,
        ).reshape(cap, rows, tb_dev, BLOCK)
        partial = combos.at[slot_row, :, train_row, :].get(mode="promise_in_bounds") * score_scale
        partial = jnp.where(live[:, None, None], partial, 0.0)
        partial = partial.reshape(n_layer, n_rep, per_dev, rows, BLOCK)
        partial = ring_reduce_scatter(partial, "layer", 0)
        got_rows = [lax.dynamic_index_in_dim(partial, rep_index, axis=0, keepdims=False)]
        for k in range(1, n_rep):
            perm = [(i, (i + k) % n_rep) for i in range(n_rep)]
            send = lax.dynamic_index_in_dim(partial, (rep_index + k) % n_rep, axis=0, keepdims=False)
            got_rows.append(lax.ppermute(send, "rep", perm))
        for k, got in enumerate(got_rows):
            owner = (rep_index - k + n_rep) % n_rep
            out_buf = lax.dynamic_update_slice(out_buf, got, (0, owner * own_rows + row_start - rows, 0))
    return out_buf.reshape(per_dev * BLOCK, BLOCK)[None]


def solution(mesh):
    placed = (
        P("groups", "layer", "span"),
        P(("groups", "span"), "layer", None),
        P("layer", "span"),
        P("groups", None),
        P(("groups", "span"), None),
        P(("groups", "span"), None),
        P(("groups", "span"), None),
    )

    return jax.shard_map(
        shards,
        mesh=mesh,
        in_specs=placed,
        out_specs=P(("groups", "span"), ("layer", "rep"), None),
        check_vma=False,
    )
```

```python
import math

import jax
import jax.numpy as jnp
from jax import lax
from jax.sharding import PartitionSpec as P


BLOCK = 128
ROW_SPLIT = (8, 24, 32)
GATE_FROM = {2: 0}


def shards(queries, train_grads, precond, requests, pair_slot, pair_train, pair_count):
    n_query, l_dev, features = queries.shape
    n_span = lax.axis_size("span")
    n_rep = lax.axis_size("rep")
    n_layer = lax.axis_size("layer")
    n_train, _, d_full = train_grads.shape
    tb_dev = n_train // BLOCK
    pmax = pair_slot.shape[1]
    cap = requests.shape[1]
    phalf = pmax // pair_count.shape[1]
    per_dev = pmax // (n_layer * n_rep)
    rep_index = lax.axis_index("rep")
    span_index = lax.axis_index("span")
    own_rows = BLOCK // n_rep

    dests = (span_index + jnp.arange(n_span, dtype=jnp.int32)) % n_span
    sources = (span_index - jnp.arange(n_span, dtype=jnp.int32) + n_span) % n_span
    t_parts = []
    for layer in range(l_dev):
        t_l = train_grads[:, layer, :]
        for k in range(n_span):
            t_parts.append(lax.dynamic_slice_in_dim(t_l, sources[k] * features, features, axis=1))
    train_local = jnp.concatenate([t_parts[layer * n_span] for layer in range(l_dev)], axis=1)
    train_remote = jnp.concatenate([p for i, p in enumerate(t_parts) if i % n_span], axis=1)

    score_scale = 1.0 / math.sqrt(l_dev * n_layer * d_full)
    slot_row = pair_slot[0]
    train_row = pair_train[0]
    counts = pair_count[0]
    slots = jnp.arange(pmax, dtype=jnp.int32)
    live = (slots % phalf) < counts[slots // phalf]

    out_buf = jnp.zeros((per_dev, BLOCK, BLOCK), jnp.float32)
    gate = None
    arrivals = []
    row_start = 0
    for chunk, rows in enumerate(ROW_SPLIT):
        block_ids = requests[dests].reshape(-1)
        if gate is not None:
            block_ids, _ = lax.optimization_barrier((block_ids, prev_sent))
        sent = []
        for layer in range(l_dev):
            q3 = queries[:, layer, :].reshape(n_query // BLOCK, BLOCK, features)
            q3 = lax.dynamic_slice_in_dim(q3, rep_index * own_rows + row_start, rows, axis=1)
            got = jnp.take(q3, block_ids, axis=0, mode="clip").reshape(n_span, cap, rows, features)
            sent.append((got.astype(jnp.float32) * precond[layer]).astype(jnp.bfloat16))
        row_start += rows
        prev_sent = sent
        if chunk in GATE_FROM:
            sent, _ = lax.optimization_barrier((sent, arrivals[GATE_FROM[chunk]]))
        pieces = []
        for layer in range(l_dev):
            for k in range(n_span):
                piece = sent[layer][k]
                if k:
                    perm = [(i, (i + k) % n_span) for i in range(n_span)]
                    piece = lax.ppermute(piece, "span", perm)
                pieces.append(piece)
        gate = pieces
        arrivals.append(pieces)
        dims = (((1,), (1,)), ((), ()))
        local = jnp.concatenate([pieces[layer * n_span] for layer in range(l_dev)], axis=-1)
        combos = lax.dot_general(local.reshape(cap * rows, -1), train_local, dims, preferred_element_type=jnp.float32)
        arrived = jnp.concatenate([p for i, p in enumerate(pieces) if i % n_span], axis=-1)
        combos = combos + lax.dot_general(
            arrived.reshape(cap * rows, -1), train_remote, dims, preferred_element_type=jnp.float32
        )
        combos = combos.reshape(cap, rows, tb_dev, BLOCK)
        partial = combos.at[slot_row, :, train_row, :].get(mode="promise_in_bounds") * score_scale
        partial = jnp.where(live[:, None, None], partial, 0.0)
        partial = partial.reshape(n_layer, n_rep, per_dev, rows, BLOCK)
        n_group = n_layer * n_rep
        me = lax.axis_index("layer") * n_rep + rep_index
        flat = partial.reshape(n_group, per_dev, rows, BLOCK)
        got = [lax.dynamic_index_in_dim(flat, me, axis=0, keepdims=False)]
        for k in range(1, n_group):
            perm = [(i, (i + k) % n_group) for i in range(n_group)]
            send = lax.dynamic_index_in_dim(flat, (me + k) % n_group, axis=0, keepdims=False)
            got.append(lax.ppermute(send, ("layer", "rep"), perm))
        stacked = jnp.stack(got, axis=0)
        row_owner = ((me - jnp.arange(n_group, dtype=jnp.int32) + n_group) % n_group) % n_rep
        for h in range(n_rep):
            rows_h = jnp.sum(jnp.where((row_owner == h)[:, None, None, None], stacked, 0.0), axis=0)
            out_buf = lax.dynamic_update_slice(out_buf, rows_h, (0, h * own_rows + row_start - rows, 0))
    return out_buf.reshape(per_dev * BLOCK, BLOCK)[None]


def solution(mesh):
    placed = (
        P("groups", "layer", "span"),
        P(("groups", "span"), "layer", None),
        P("layer", "span"),
        P("groups", None),
        P(("groups", "span"), None),
        P(("groups", "span"), None),
        P(("groups", "span"), None),
    )

    return jax.shard_map(
        shards,
        mesh=mesh,
        in_specs=placed,
        out_specs=P(("groups", "span"), ("layer", "rep"), None),
        check_vma=False,
    )
```

```python
import math

import jax
import jax.numpy as jnp
from jax import lax
from jax.sharding import PartitionSpec as P


BLOCK = 128
ROW_SPLIT = (8, 24, 32)
GATE_FROM = {2: 0}


def shards(queries, train_grads, precond, requests, pair_slot, pair_train, pair_count):
    n_query, l_dev, features = queries.shape
    n_span = lax.axis_size("span")
    n_rep = lax.axis_size("rep")
    n_layer = lax.axis_size("layer")
    n_train, _, d_full = train_grads.shape
    tb_dev = n_train // BLOCK
    pmax = pair_slot.shape[1]
    cap = requests.shape[1]
    phalf = pmax // pair_count.shape[1]
    per_dev = pmax // (n_layer * n_rep)
    rep_index = lax.axis_index("rep")
    span_index = lax.axis_index("span")
    own_rows = BLOCK // n_rep

    dests = (span_index + jnp.arange(n_span, dtype=jnp.int32)) % n_span
    sources = (span_index - jnp.arange(n_span, dtype=jnp.int32) + n_span) % n_span
    t_parts = []
    for layer in range(l_dev):
        t_l = train_grads[:, layer, :]
        for k in range(n_span):
            t_parts.append(lax.dynamic_slice_in_dim(t_l, sources[k] * features, features, axis=1))
    train = jnp.concatenate(t_parts, axis=1)

    score_scale = 1.0 / math.sqrt(l_dev * n_layer * d_full)
    slot_row = pair_slot[0]
    train_row = pair_train[0]
    counts = pair_count[0]
    slots = jnp.arange(pmax, dtype=jnp.int32)
    live = (slots % phalf) < counts[slots // phalf]

    out_buf = jnp.zeros((per_dev, BLOCK, BLOCK), jnp.float32)
    gate = None
    arrivals = []
    row_start = 0
    for chunk, rows in enumerate(ROW_SPLIT):
        block_ids = requests[dests].reshape(-1)
        if gate is not None:
            block_ids, _ = lax.optimization_barrier((block_ids, prev_sent))
        sent = []
        for layer in range(l_dev):
            q3 = queries[:, layer, :].reshape(n_query // BLOCK, BLOCK, features)
            q3 = lax.dynamic_slice_in_dim(q3, rep_index * own_rows + row_start, rows, axis=1)
            got = jnp.take(q3, block_ids, axis=0, mode="clip").reshape(n_span, cap, rows, features)
            sent.append((got.astype(jnp.float32) * precond[layer]).astype(jnp.bfloat16))
        row_start += rows
        prev_sent = sent
        if chunk in GATE_FROM:
            sent, _ = lax.optimization_barrier((sent, arrivals[GATE_FROM[chunk]]))
        pieces = []
        for layer in range(l_dev):
            for k in range(n_span):
                piece = sent[layer][k]
                if k:
                    perm = [(i, (i + k) % n_span) for i in range(n_span)]
                    piece = lax.ppermute(piece, "span", perm)
                pieces.append(piece)
        gate = pieces
        arrivals.append(pieces)
        arrived = jnp.concatenate(pieces, axis=-1).reshape(cap * rows, -1)
        combos = lax.dot_general(
            arrived,
            train,
            (((1,), (1,)), ((), ())),
            preferred_element_type=jnp.float32,
        ).reshape(cap, rows, tb_dev, BLOCK)
        partial = combos.at[slot_row, :, train_row, :].get(mode="promise_in_bounds") * score_scale
        partial = jnp.where(live[:, None, None], partial, 0.0)
        partial = partial.reshape(n_layer, n_rep, per_dev, rows, BLOCK)
        n_group = n_layer * n_rep
        me = lax.axis_index("layer") * n_rep + rep_index
        flat = partial.reshape(n_group, per_dev, rows, BLOCK)
        got = [lax.dynamic_index_in_dim(flat, me, axis=0, keepdims=False)] + [None] * (n_group - 1)
        for k in range(n_group - 1, 0, -1):
            perm = [(i, (i + k) % n_group) for i in range(n_group)]
            send = lax.dynamic_index_in_dim(flat, (me + k) % n_group, axis=0, keepdims=False)
            got[k] = lax.ppermute(send, ("layer", "rep"), perm)
        stacked = jnp.stack(got, axis=0)
        row_owner = ((me - jnp.arange(n_group, dtype=jnp.int32) + n_group) % n_group) % n_rep
        for h in range(n_rep):
            rows_h = jnp.sum(jnp.where((row_owner == h)[:, None, None, None], stacked, 0.0), axis=0)
            out_buf = lax.dynamic_update_slice(out_buf, rows_h, (0, h * own_rows + row_start - rows, 0))
    return out_buf.reshape(per_dev * BLOCK, BLOCK)[None]


def solution(mesh):
    placed = (
        P("groups", "layer", "span"),
        P(("groups", "span"), "layer", None),
        P("layer", "span"),
        P("groups", None),
        P(("groups", "span"), None),
        P(("groups", "span"), None),
        P(("groups", "span"), None),
    )

    return jax.shard_map(
        shards,
        mesh=mesh,
        in_specs=placed,
        out_specs=P(("groups", "span"), ("layer", "rep"), None),
        check_vma=False,
    )
```

```python
import math

import jax
import jax.numpy as jnp
from jax import lax
from jax.sharding import PartitionSpec as P


BLOCK = 128
ROW_SPLIT = (8, 16, 40)
GATE_FROM = {2: 0}


def shards(queries, train_grads, precond, requests, pair_slot, pair_train, pair_count):
    n_query, l_dev, features = queries.shape
    n_span = lax.axis_size("span")
    n_rep = lax.axis_size("rep")
    n_layer = lax.axis_size("layer")
    n_train, _, d_full = train_grads.shape
    tb_dev = n_train // BLOCK
    pmax = pair_slot.shape[1]
    cap = requests.shape[1]
    phalf = pmax // pair_count.shape[1]
    per_dev = pmax // (n_layer * n_rep)
    rep_index = lax.axis_index("rep")
    span_index = lax.axis_index("span")
    own_rows = BLOCK // n_rep

    dests = (span_index + jnp.arange(n_span, dtype=jnp.int32)) % n_span
    sources = (span_index - jnp.arange(n_span, dtype=jnp.int32) + n_span) % n_span
    t_parts = []
    for layer in range(l_dev):
        t_l = train_grads[:, layer, :]
        for k in range(n_span):
            t_parts.append(lax.dynamic_slice_in_dim(t_l, sources[k] * features, features, axis=1))
    train = jnp.concatenate(t_parts, axis=1)

    score_scale = 1.0 / math.sqrt(l_dev * n_layer * d_full)
    slot_row = pair_slot[0]
    train_row = pair_train[0]
    counts = pair_count[0]
    slots = jnp.arange(pmax, dtype=jnp.int32)
    live = (slots % phalf) < counts[slots // phalf]

    out_buf = jnp.zeros((per_dev, BLOCK, BLOCK), jnp.float32)
    gate = None
    arrivals = []
    row_start = 0
    for chunk, rows in enumerate(ROW_SPLIT):
        block_ids = requests[dests].reshape(-1)
        if gate is not None:
            block_ids, _ = lax.optimization_barrier((block_ids, prev_sent))
        sent = []
        for layer in range(l_dev):
            q3 = queries[:, layer, :].reshape(n_query // BLOCK, BLOCK, features)
            q3 = lax.dynamic_slice_in_dim(q3, rep_index * own_rows + row_start, rows, axis=1)
            got = jnp.take(q3, block_ids, axis=0, mode="clip").reshape(n_span, cap, rows, features)
            sent.append((got.astype(jnp.float32) * precond[layer]).astype(jnp.bfloat16))
        row_start += rows
        prev_sent = sent
        if chunk in GATE_FROM:
            sent, _ = lax.optimization_barrier((sent, arrivals[GATE_FROM[chunk]]))
        pieces = []
        for layer in range(l_dev):
            for k in range(n_span):
                piece = sent[layer][k]
                if k:
                    perm = [(i, (i + k) % n_span) for i in range(n_span)]
                    piece = lax.ppermute(piece, "span", perm)
                pieces.append(piece)
        gate = pieces
        arrivals.append(pieces)
        arrived = jnp.concatenate(pieces, axis=-1).reshape(cap * rows, -1)
        combos = lax.dot_general(
            arrived,
            train,
            (((1,), (1,)), ((), ())),
            preferred_element_type=jnp.float32,
        ).reshape(cap, rows, tb_dev, BLOCK)
        partial = combos.at[slot_row, :, train_row, :].get(mode="promise_in_bounds") * score_scale
        partial = jnp.where(live[:, None, None], partial, 0.0)
        partial = partial.reshape(n_layer, n_rep, per_dev, rows, BLOCK)
        n_group = n_layer * n_rep
        me = lax.axis_index("layer") * n_rep + rep_index
        flat = partial.reshape(n_group, per_dev, rows, BLOCK)
        got = [lax.dynamic_index_in_dim(flat, me, axis=0, keepdims=False)]
        for k in range(1, n_group):
            perm = [(i, (i + k) % n_group) for i in range(n_group)]
            send = lax.dynamic_index_in_dim(flat, (me + k) % n_group, axis=0, keepdims=False)
            got.append(lax.ppermute(send, ("layer", "rep"), perm))
        stacked = jnp.stack(got, axis=0)
        row_owner = ((me - jnp.arange(n_group, dtype=jnp.int32) + n_group) % n_group) % n_rep
        for h in range(n_rep):
            rows_h = jnp.sum(jnp.where((row_owner == h)[:, None, None, None], stacked, 0.0), axis=0)
            out_buf = lax.dynamic_update_slice(out_buf, rows_h, (0, h * own_rows + row_start - rows, 0))
    return out_buf.reshape(per_dev * BLOCK, BLOCK)[None]


def solution(mesh):
    placed = (
        P("groups", "layer", "span"),
        P(("groups", "span"), "layer", None),
        P("layer", "span"),
        P("groups", None),
        P(("groups", "span"), None),
        P(("groups", "span"), None),
        P(("groups", "span"), None),
    )

    return jax.shard_map(
        shards,
        mesh=mesh,
        in_specs=placed,
        out_specs=P(("groups", "span"), ("layer", "rep"), None),
        check_vma=False,
    )
```
